512 devices in a mesh: ctxlo: 16 (over z_hi, x), ctxhi: 32 (over y, z_lo, core).
Axes of the slice: x: 4, y: 8, z: 8 (z_hi: 4, z_lo: 2; z = z_hi * 2 + z_lo), core: 2. Of those that a mesh axis runs over, the one named last changes fastest.
Arguments:
- key_value: bfloat16 [32, 16, 384, 256], P('ctxhi', 'ctxlo'), may hold values from -6 to 6
- queries: bfloat16 [32, 16, 384, 768], P('ctxhi', 'ctxlo'), may hold values from -300 to 300
Outputs:
- attended: bfloat16 [32, 16, 384, 768], P('ctxhi', 'ctxlo')
The draws below stay inside these ranges and needn't reach their ends.
All inputs are finite; a program needn't handle non-finite values.
Results may differ from the reference program's by a relative error of at most 0.0038.
Values may be sent and summed in bfloat16 or wider, within the bound.
No kernel may reach another device: no remote copies, remote signals or barrier semaphores. Data moves between devices by JAX's collectives and lax.ppermute only.
A program may use at most 64 MiB of HBM per device.

```python
import math
import jax
import jax.numpy as jnp
from jax import lax

HD = 128
HQ = 6
TOK_DEV = 384
N_CTXLO = 16
N_CTXHI = 32


def draw_queries(key, part):
    first = jax.random.fold_in(jax.random.fold_in(key, 7), 0)
    shape = (N_CTXHI, N_CTXLO, TOK_DEV, HQ * HD)
    base = jnp.clip(jax.random.normal(first, shape, jnp.float32), -5.0, 5.0) * 3.0
    return base.astype(jnp.bfloat16)


def block_scale(key, extent, pieces, least, high):
    level = 1.0
    for axis_at, blocks in pieces:
        draws = jax.random.uniform(jax.random.fold_in(jax.random.fold_in(key, 6), axis_at), (blocks,), jnp.float32, least / len(pieces), high / len(pieces))
        level = level * jnp.repeat(jnp.exp(draws), extent[axis_at] // blocks).reshape((-1,) + (1,) * (len(extent) - 1 - axis_at))
    return level


def noise(key, shape, spread, reach, cuts=(), kind=jnp.bfloat16):
    loudness = block_scale(key, shape, cuts, -0.22, 0.18) if cuts else 1.0
    values = jax.random.normal(key, shape, jnp.float32) * spread * loudness
    return jnp.minimum(jnp.maximum(values, -reach), reach).astype(kind)


def setup_inputs(seed: int = 0) -> dict:
    splits = jax.random.split(jax.random.key(seed), 3)
    key_value = noise(splits[0], (N_CTXHI, N_CTXLO, TOK_DEV, 2 * HD), 1.0, 6.0, ((0, 32), (1, 16)))
    queries = draw_queries(jax.random.fold_in(splits[2], 71), 0)
    return {"key_value": key_value, "queries": queries}


def reference(key_value, queries):
    blocks = N_CTXHI * N_CTXLO
    kv_all = key_value.reshape(blocks, TOK_DEV, 2 * HD)
    query_all = queries.reshape(blocks, TOK_DEV, HQ, HD)
    nbits = blocks.bit_length() - 1
    powers = jnp.array([0] + [1 << b for b in range(nbits)], dtype=jnp.int32)
    scale = 1.0 / math.sqrt(HD)

    def attend(args):
        index, query = args
        visible = jnp.bitwise_xor(index, powers).astype(jnp.int32)
        gathered = jnp.take(kv_all, visible, axis=0).reshape(-1, 2 * HD)
        keys = gathered[:, :HD].astype(jnp.float32)
        values = gathered[:, HD:].astype(jnp.float32)
        scores = jnp.einsum('thd,sd->hts', query.astype(jnp.float32), keys) * scale
        top = lax.optimization_barrier(jnp.max(scores, axis=-1, keepdims=True))
        expo = jnp.exp(scores - top)
        total = lax.optimization_barrier(jnp.sum(expo, axis=-1))
        weights = expo.astype(jnp.bfloat16).astype(jnp.float32)
        summed = jnp.einsum('hts,sd->thd', weights, values)
        result = summed / jnp.transpose(total)[:, :, None]
        return result.astype(jnp.bfloat16).reshape(TOK_DEV, HQ * HD)
    result = lax.map(attend, (jnp.arange(blocks, dtype=jnp.int32), query_all))
    return result.reshape(N_CTXHI, N_CTXLO, TOK_DEV, HQ * HD)
```

```python
import math

import jax
import jax.numpy as jnp
from jax import lax
from jax.experimental import pallas as pl
from jax.experimental.pallas import tpu as pltpu
from jax.sharding import PartitionSpec as P

HQ = 6


def swapped(block, axis, stride):
    count = lax.axis_size(axis)
    route = []
    for low in range(count):
        high = low | 1 << stride
        if high != low and high < count:
            route += [(low, high), (high, low)]
    return lax.ppermute(block, axis, route)


def attend_kernel(*refs):
    q_ref = refs[0]
    kv_refs = refs[1:-2]
    o_ref, s_ref = refs[-2], refs[-1]
    tokens = q_ref.shape[0]
    head_size = q_ref.shape[1]
    scale = 1.0 / math.sqrt(head_size)
    query = q_ref[...]
    for j, kv_ref in enumerate(kv_refs):
        keys = kv_ref[:, :head_size]
        scores = lax.dot_general(
            query, keys, (((1,), (1,)), ((), ())), preferred_element_type=jnp.float32
        )
        s_ref[:, j * tokens:(j + 1) * tokens] = scores * scale
    scores = s_ref[...]
    top = jnp.max(scores, axis=-1, keepdims=True)
    expo = jnp.exp(scores - top)
    total = jnp.sum(expo, axis=-1, keepdims=True)
    weights = expo.astype(jnp.bfloat16)
    summed = jnp.zeros((tokens, head_size), jnp.float32)
    for j, kv_ref in enumerate(kv_refs):
        summed = summed + jnp.dot(
            weights[:, j * tokens:(j + 1) * tokens],
            kv_ref[:, head_size:],
            preferred_element_type=jnp.float32,
        )
    o_ref[...] = (summed / total).astype(o_ref.dtype)


def attend(query, blocks):
    tokens, width = query.shape
    head_size = blocks[0].shape[1] // 2
    kv_spec = pl.BlockSpec(blocks[0].shape, lambda h: (0, 0))
    return pl.pallas_call(
        attend_kernel,
        out_shape=jax.ShapeDtypeStruct((tokens, width), jnp.bfloat16),
        grid=(width // head_size,),
        in_specs=[pl.BlockSpec((tokens, head_size), lambda h: (0, h))] + [kv_spec] * len(blocks),
        out_specs=pl.BlockSpec((tokens, head_size), lambda h: (0, h)),
        scratch_shapes=[pltpu.VMEM((tokens, tokens * len(blocks)), jnp.float32)],
    )(query, *blocks)


def per_device(key_value, queries):
    tokens = key_value.shape[2]
    pair = key_value.shape[3]
    local_kv = key_value.reshape(tokens, pair)
    query = queries.reshape(tokens, queries.shape[3])
    blocks = [local_kv]
    for bit in range(lax.axis_size("ctxlo").bit_length() - 1):
        blocks.append(swapped(local_kv, "ctxlo", bit))
    for bit in range(lax.axis_size("ctxhi").bit_length() - 1):
        blocks.append(swapped(local_kv, "ctxhi", bit))
    result = attend(query, blocks)
    return result.reshape(1, 1, tokens, queries.shape[3])


def solution(mesh):
    return jax.shard_map(
        per_device,
        mesh=mesh,
        in_specs=(P("ctxhi", "ctxlo", None, None), P("ctxhi", "ctxlo", None, None)),
        out_specs=P("ctxhi", "ctxlo", None, None),
        check_vma=False,
    )
```

```python
import math

import jax
import jax.numpy as jnp
from jax import lax
from jax.experimental import pallas as pl
from jax.experimental.pallas import tpu as pltpu
from jax.sharding import Mesh, PartitionSpec as P

HQ = 6


def bit_names(prefix, count):
    return tuple(f"{prefix}{b}" for b in reversed(range(count.bit_length() - 1)))


def attend_kernel(sel_ref, *refs):
    q_ref = refs[0]
    kv_refs = refs[1:-2]
    o_ref, s_ref = refs[-2], refs[-1]
    tokens = q_ref.shape[0]
    head_size = q_ref.shape[1]
    scale = 1.0 / math.sqrt(head_size)
    query = q_ref[...]
    for j, kv_ref in enumerate(kv_refs):
        keys = kv_ref[:, :head_size]
        scores = lax.dot_general(
            query, keys, (((1,), (1,)), ((), ())), preferred_element_type=jnp.float32
        )
        s_ref[:, j * tokens:(j + 1) * tokens] = scores * scale
    scores = s_ref[...]
    top = jnp.max(scores, axis=-1, keepdims=True)
    expo = jnp.exp(scores - top)
    total = jnp.sum(expo, axis=-1, keepdims=True)
    weights = expo.astype(jnp.bfloat16)
    summed = jnp.zeros((tokens, head_size), jnp.float32)
    for j, kv_ref in enumerate(kv_refs):
        summed = summed + jnp.dot(
            weights[:, j * tokens:(j + 1) * tokens],
            kv_ref[:, head_size:],
            preferred_element_type=jnp.float32,
        )
    o_ref[...] = (summed / total).astype(o_ref.dtype)


def attend(query, local, picks):
    tokens, width = query.shape
    head_size = local.shape[1] // 2
    sel = jnp.stack([index for _, index in picks]).astype(jnp.int32)
    local_spec = pl.BlockSpec(local.shape, lambda h, s: (0, 0))
    specs = [pl.BlockSpec((tokens, head_size), lambda h, s: (0, h)), local_spec]
    for i, _ in enumerate(picks):
        specs.append(pl.BlockSpec((None,) + local.shape, lambda h, s, i=i: (s[i], 0, 0)))
    grid_spec = pltpu.PrefetchScalarGridSpec(
        num_scalar_prefetch=1,
        grid=(width // head_size,),
        in_specs=specs,
        out_specs=pl.BlockSpec((tokens, head_size), lambda h, s: (0, h)),
        scratch_shapes=[pltpu.VMEM((tokens, tokens * (len(picks) + 1)), jnp.float32)],
    )
    return pl.pallas_call(
        attend_kernel,
        out_shape=jax.ShapeDtypeStruct((tokens, width), jnp.bfloat16),
        grid_spec=grid_spec,
    )(sel, query, local, *[gathered for gathered, _ in picks])


def make_per_device(groups):
    def per_device(key_value, queries):
        tokens = key_value.shape[2]
        pair = key_value.shape[3]
        local_kv = key_value.reshape(tokens, pair)
        query = queries.reshape(tokens, queries.shape[3])
        picks = []
        for names in groups:
            gathered = lax.all_gather(local_kv, names)
            me = lax.axis_index(names)
            for b in range(len(names)):
                picks.append((gathered, jnp.bitwise_xor(me, 1 << b)))
        result = attend(query, local_kv, picks)
        return result.reshape(1, 1, tokens, queries.shape[3])
    return per_device


def solution(mesh):
    hi = bit_names("h", mesh.shape["ctxhi"])
    lo = bit_names("l", mesh.shape["ctxlo"])
    names = {"ctxhi": hi, "ctxlo": lo}
    order = sum((names[axis] for axis in mesh.axis_names), ())
    binary = Mesh(mesh.devices.reshape((2,) * len(order)), order)
    groups = [lo[i:i + 2] for i in range(0, len(lo), 2)]
    groups += [hi[::-1][i:i + 2][::-1] for i in range(0, len(hi), 2)]
    spec = P(hi, lo, None, None)
    return jax.shard_map(
        make_per_device(groups),
        mesh=binary,
        in_specs=(spec, spec),
        out_specs=spec,
        check_vma=False,
    )
```

```python
import math

import jax
import jax.numpy as jnp
from jax import lax
from jax.experimental import pallas as pl
from jax.experimental.pallas import tpu as pltpu
from jax.sharding import Mesh, PartitionSpec as P

HQ = 6
OFFLOADED = ("l",)


def bit_names(prefix, count):
    return tuple(f"{prefix}{b}" for b in reversed(range(count.bit_length() - 1)))


def lane_fold(x, op):
    parts = [x[:, c * 128:(c + 1) * 128] for c in range(x.shape[1] // 128)]
    out = parts[0]
    for part in parts[1:]:
        out = op(out, part)
    return out


def attend_kernel(sel_ref, *refs):
    q_ref = refs[0]
    kv_refs = refs[1:-2]
    o_ref, s_ref = refs[-2], refs[-1]
    tokens = q_ref.shape[0]
    head_size = kv_refs[0].shape[-1] // 2
    heads = q_ref.shape[1] // head_size
    scale = 1.0 / math.sqrt(head_size)
    query = jnp.concatenate(
        [q_ref[:, h * head_size:(h + 1) * head_size] for h in range(heads)], axis=0
    )
    part_top = None
    for j, kv_ref in enumerate(kv_refs):
        scores = lax.dot_general(
            query, kv_ref[:, :head_size], (((1,), (1,)), ((), ())),
            preferred_element_type=jnp.float32,
        )
        s_ref[j] = scores
        folded = lane_fold(scores, jnp.maximum)
        part_top = folded if part_top is None else jnp.maximum(part_top, folded)
    top = jnp.max(part_top, axis=-1, keepdims=True)
    summed = None
    part_total = None
    for j, kv_ref in enumerate(kv_refs):
        expo = jnp.exp((s_ref[j] - top) * scale)
        folded = lane_fold(expo, jnp.add)
        part_total = folded if part_total is None else part_total + folded
        update = jnp.dot(
            expo.astype(jnp.bfloat16), kv_ref[:, head_size:],
            preferred_element_type=jnp.float32,
        )
        summed = update if summed is None else summed + update
    total = jnp.sum(part_total, axis=-1, keepdims=True)
    result = (summed / total).astype(o_ref.dtype)
    for h in range(heads):
        o_ref[:, h * head_size:(h + 1) * head_size] = result[h * tokens:(h + 1) * tokens]


def attend(query, picks):
    tokens, width = query.shape
    block = picks[0][0].shape[1:]
    rows = tokens * (width // (block[1] // 2))
    sel = jnp.stack([index for _, index in picks]).astype(jnp.int32)
    specs = [pl.BlockSpec((tokens, width), lambda i, s: (0, 0))]
    for n, _ in enumerate(picks):
        specs.append(pl.BlockSpec((None,) + block, lambda i, s, n=n: (s[n], 0, 0)))
    grid_spec = pltpu.PrefetchScalarGridSpec(
        num_scalar_prefetch=1,
        grid=(1,),
        in_specs=specs,
        out_specs=pl.BlockSpec((tokens, width), lambda i, s: (0, 0)),
        scratch_shapes=[pltpu.VMEM((len(picks), rows, tokens), jnp.float32)],
    )
    return pl.pallas_call(
        attend_kernel,
        out_shape=jax.ShapeDtypeStruct((tokens, width), jnp.bfloat16),
        grid_spec=grid_spec,
    )(sel, query, *[stacked for stacked, _ in picks])


def exchange(local, name):
    me = lax.axis_index(name)
    if name[0] in OFFLOADED:
        slots = jnp.zeros((2,) + local.shape, local.dtype)
        slots = lax.dynamic_update_index_in_dim(slots, local, me, 0)
        return lax.psum(slots, name), 1 - me
    return lax.ppermute(local, name, [(0, 1), (1, 0)])[None], jnp.zeros((), jnp.int32)


def make_per_device(names):
    def per_device(key_value, queries):
        tokens = key_value.shape[2]
        pair = key_value.shape[3]
        local_kv = key_value.reshape(tokens, pair)
        query = queries.reshape(tokens, queries.shape[3])
        picks = [(local_kv[None], jnp.zeros((), jnp.int32))]
        for name in names:
            picks.append(exchange(local_kv, name))
        result = attend(query, picks)
        return result.reshape(1, 1, tokens, queries.shape[3])
    return per_device


def solution(mesh):
    hi = bit_names("h", mesh.shape["ctxhi"])
    lo = bit_names("l", mesh.shape["ctxlo"])
    names = {"ctxhi": hi, "ctxlo": lo}
    order = sum((names[axis] for axis in mesh.axis_names), ())
    binary = Mesh(mesh.devices.reshape((2,) * len(order)), order)
    spec = P(hi, lo, None, None)
    return jax.shard_map(
        make_per_device(lo[::-1] + hi[::-1]),
        mesh=binary,
        in_specs=(spec, spec),
        out_specs=spec,
        check_vma=False,
    )
```

```python
import math

import jax
import jax.numpy as jnp
from jax import lax
from jax.experimental import pallas as pl
from jax.sharding import PartitionSpec as P

HQ = 6
LAUNCH_ORDER = (
    ("ctxhi", 4), ("ctxlo", 3), ("ctxhi", 3), ("ctxlo", 2), ("ctxlo", 1),
    ("ctxhi", 2), ("ctxhi", 1), ("ctxlo", 0), ("ctxhi", 0),
)
LATE_BLOCKS = 3


def swapped(block, axis, stride):
    count = lax.axis_size(axis)
    route = []
    for low in range(count):
        high = low | 1 << stride
        if high != low and high < count:
            route += [(low, high), (high, low)]
    return lax.ppermute(block, axis, route)


def stacked_query(q_ref, head_size):
    heads = q_ref.shape[1] // head_size
    return jnp.concatenate(
        [q_ref[:, h * head_size:(h + 1) * head_size] for h in range(heads)], axis=0
    )


def block_scores(kv_refs, query, head_size):
    return [
        lax.dot_general(
            kv_ref[:, :head_size], query, (((1,), (1,)), ((), ())),
            preferred_element_type=jnp.float32,
        )
        for kv_ref in kv_refs
    ]


def absorb(kv_refs, scores, top, head_size):
    factor = math.log2(math.e) / math.sqrt(head_size)
    summed = None
    total = None
    for kv_ref, block in zip(kv_refs, scores):
        expo = jnp.exp2((block - top) * factor)
        block_total = jnp.sum(expo, axis=0, keepdims=True)
        total = block_total if total is None else total + block_total
        update = lax.dot_general(
            kv_ref[:, head_size:], expo.astype(jnp.bfloat16), (((0,), (0,)), ((), ())),
            preferred_element_type=jnp.float32,
        )
        summed = update if summed is None else summed + update
    return summed, total


def row_max(scores):
    top = None
    for block in scores:
        block_top = jnp.max(block, axis=0, keepdims=True)
        top = block_top if top is None else jnp.maximum(top, block_top)
    return top


def first_kernel(*refs):
    q_ref = refs[0]
    kv_refs = refs[1:-3]
    summed_ref, top_ref, total_ref = refs[-3:]
    head_size = kv_refs[0].shape[1] // 2
    scores = block_scores(kv_refs, stacked_query(q_ref, head_size), head_size)
    top = row_max(scores)
    summed, total = absorb(kv_refs, scores, top, head_size)
    summed_ref[...] = summed
    top_ref[...] = top
    total_ref[...] = total


def last_kernel(*refs):
    q_ref, summed_ref, top_ref, total_ref = refs[:4]
    kv_refs = refs[4:-1]
    o_ref = refs[-1]
    tokens = q_ref.shape[0]
    head_size = kv_refs[0].shape[1] // 2
    heads = q_ref.shape[1] // head_size
    factor = math.log2(math.e) / math.sqrt(head_size)
    scores = block_scores(kv_refs, stacked_query(q_ref, head_size), head_size)
    first_top = top_ref[...]
    top = jnp.maximum(first_top, row_max(scores))
    fade = jnp.exp2((first_top - top) * factor)
    summed, total = absorb(kv_refs, scores, top, head_size)
    summed = summed + summed_ref[...] * fade
    total = total + total_ref[...] * fade
    result = (summed / total).T.astype(o_ref.dtype)
    for h in range(heads):
        o_ref[:, h * head_size:(h + 1) * head_size] = result[h * tokens:(h + 1) * tokens]


def whole(shape):
    return pl.BlockSpec(shape, lambda i: (0,) * len(shape))


def attend(query, first, last):
    tokens, width = query.shape
    head_size = first[0].shape[1] // 2
    rows = tokens * (width // head_size)
    state = [
        jax.ShapeDtypeStruct((head_size, rows), jnp.float32),
        jax.ShapeDtypeStruct((1, rows), jnp.float32),
        jax.ShapeDtypeStruct((1, rows), jnp.float32),
    ]
    kv_spec = whole(first[0].shape)
    state_specs = [whole(part.shape) for part in state]
    partial = pl.pallas_call(
        first_kernel,
        out_shape=state,
        grid=(1,),
        in_specs=[whole(query.shape)] + [kv_spec] * len(first),
        out_specs=state_specs,
    )(query, *first)
    return pl.pallas_call(
        last_kernel,
        out_shape=jax.ShapeDtypeStruct((tokens, width), jnp.bfloat16),
        grid=(1,),
        in_specs=[whole(query.shape)] + state_specs + [kv_spec] * len(last),
        out_specs=whole(query.shape),
    )(query, *partial, *last)


def per_device(key_value, queries):
    tokens = key_value.shape[2]
    pair = key_value.shape[3]
    local_kv = key_value.reshape(tokens, pair)
    query = queries.reshape(tokens, queries.shape[3])
    received = [swapped(local_kv, axis, bit) for axis, bit in LAUNCH_ORDER[::-1]][::-1]
    split = len(received) - LATE_BLOCKS
    result = attend(query, [local_kv] + received[:split], received[split:])
    return result.reshape(1, 1, tokens, queries.shape[3])


def solution(mesh):
    return jax.shard_map(
        per_device,
        mesh=mesh,
        in_specs=(P("ctxhi", "ctxlo", None, None), P("ctxhi", "ctxlo", None, None)),
        out_specs=P("ctxhi", "ctxlo", None, None),
        check_vma=False,
    )
```

```python
import math

import jax
import jax.numpy as jnp
from jax import lax
from jax.experimental import pallas as pl
from jax.sharding import PartitionSpec as P

HQ = 6
LAUNCH_ORDER = (
    ("ctxhi", 4), ("ctxlo", 3), ("ctxhi", 3), ("ctxlo", 2), ("ctxhi", 0),
    ("ctxlo", 1), ("ctxhi", 2), ("ctxhi", 1), ("ctxlo", 0),
)


def swapped(block, axis, stride):
    count = lax.axis_size(axis)
    route = []
    for low in range(count):
        high = low | 1 << stride
        if high != low and high < count:
            route += [(low, high), (high, low)]
    return lax.ppermute(block, axis, route)


def attend_kernel(*refs):
    q_ref = refs[0]
    kv_refs = refs[1:-1]
    o_ref = refs[-1]
    tokens = q_ref.shape[0]
    head_size = kv_refs[0].shape[1] // 2
    heads = q_ref.shape[1] // head_size
    scale = 1.0 / math.sqrt(head_size)
    query = jnp.concatenate(
        [q_ref[:, h * head_size:(h + 1) * head_size] for h in range(heads)], axis=0
    )
    scores = []
    top = None
    for kv_ref in kv_refs:
        block = lax.dot_general(
            kv_ref[:, :head_size], query, (((1,), (1,)), ((), ())),
            preferred_element_type=jnp.float32,
        )
        scores.append(block)
        block_top = jnp.max(block, axis=0, keepdims=True)
        top = block_top if top is None else jnp.maximum(top, block_top)
    summed = None
    total = None
    for kv_ref, block in zip(kv_refs, scores):
        expo = jnp.exp2((block - top) * (scale * math.log2(math.e)))
        block_total = jnp.sum(expo, axis=0, keepdims=True)
        total = block_total if total is None else total + block_total
        update = lax.dot_general(
            kv_ref[:, head_size:], expo.astype(jnp.bfloat16), (((0,), (0,)), ((), ())),
            preferred_element_type=jnp.float32,
        )
        summed = update if summed is None else summed + update
    result = (summed / total).T.astype(o_ref.dtype)
    for h in range(heads):
        o_ref[:, h * head_size:(h + 1) * head_size] = result[h * tokens:(h + 1) * tokens]


def attend(query, blocks):
    tokens, width = query.shape
    kv_spec = pl.BlockSpec(blocks[0].shape, lambda i: (0, 0))
    return pl.pallas_call(
        attend_kernel,
        out_shape=jax.ShapeDtypeStruct((tokens, width), jnp.bfloat16),
        grid=(1,),
        in_specs=[pl.BlockSpec((tokens, width), lambda i: (0, 0))] + [kv_spec] * len(blocks),
        out_specs=pl.BlockSpec((tokens, width), lambda i: (0, 0)),
    )(query, *blocks)


def per_device(key_value, queries):
    tokens = key_value.shape[2]
    pair = key_value.shape[3]
    local_kv = key_value.reshape(tokens, pair)
    query = queries.reshape(tokens, queries.shape[3])
    blocks = [local_kv]
    for axis, bit in LAUNCH_ORDER[::-1]:
        blocks.append(swapped(local_kv, axis, bit))
    result = attend(query, blocks)
    return result.reshape(1, 1, tokens, queries.shape[3])


def solution(mesh):
    return jax.shard_map(
        per_device,
        mesh=mesh,
        in_specs=(P("ctxhi", "ctxlo", None, None), P("ctxhi", "ctxlo", None, None)),
        out_specs=P("ctxhi", "ctxlo", None, None),
        check_vma=False,
    )
```

```python
import math

import jax
import jax.numpy as jnp
from jax import lax
from jax.experimental import pallas as pl
from jax.sharding import PartitionSpec as P

HQ = 6
LAUNCH_ORDER = (
    ("ctxhi", 4), ("ctxhi", 3), ("ctxlo", 3), ("ctxlo", 2), ("ctxlo", 1),
    ("ctxhi", 2), ("ctxhi", 1), ("ctxlo", 0), ("ctxhi", 0),
)


def swapped(block, axis, stride):
    count = lax.axis_size(axis)
    route = []
    for low in range(count):
        high = low | 1 << stride
        if high != low and high < count:
            route += [(low, high), (high, low)]
    return lax.ppermute(block, axis, route)


def attend_kernel(*refs):
    q_ref = refs[0]
    kv_refs = refs[1:-1]
    o_ref = refs[-1]
    tokens = q_ref.shape[0]
    head_size = kv_refs[0].shape[1] // 2
    heads = q_ref.shape[1] // head_size
    scale = 1.0 / math.sqrt(head_size)
    query = jnp.concatenate(
        [q_ref[:, h * head_size:(h + 1) * head_size] for h in range(heads)], axis=0
    )
    scores = []
    top = None
    for kv_ref in kv_refs:
        block = lax.dot_general(
            kv_ref[:, :head_size], query, (((1,), (1,)), ((), ())),
            preferred_element_type=jnp.float32,
        )
        scores.append(block)
        block_top = jnp.max(block, axis=0, keepdims=True)
        top = block_top if top is None else jnp.maximum(top, block_top)
    summed = None
    total = None
    for kv_ref, block in zip(kv_refs, scores):
        expo = jnp.exp2((block - top) * (scale * math.log2(math.e)))
        block_total = jnp.sum(expo, axis=0, keepdims=True)
        total = block_total if total is None else total + block_total
        update = lax.dot_general(
            kv_ref[:, head_size:], expo.astype(jnp.bfloat16), (((0,), (0,)), ((), ())),
            preferred_element_type=jnp.float32,
        )
        summed = update if summed is None else summed + update
    result = (summed / total).T.astype(o_ref.dtype)
    for h in range(heads):
        o_ref[:, h * head_size:(h + 1) * head_size] = result[h * tokens:(h + 1) * tokens]


def attend(query, blocks):
    tokens, width = query.shape
    kv_spec = pl.BlockSpec(blocks[0].shape, lambda i: (0, 0))
    return pl.pallas_call(
        attend_kernel,
        out_shape=jax.ShapeDtypeStruct((tokens, width), jnp.bfloat16),
        grid=(1,),
        in_specs=[pl.BlockSpec((tokens, width), lambda i: (0, 0))] + [kv_spec] * len(blocks),
        out_specs=pl.BlockSpec((tokens, width), lambda i: (0, 0)),
    )(query, *blocks)


def per_device(key_value, queries):
    tokens = key_value.shape[2]
    pair = key_value.shape[3]
    local_kv = key_value.reshape(tokens, pair)
    query = queries.reshape(tokens, queries.shape[3])
    blocks = [local_kv]
    for axis, bit in LAUNCH_ORDER[::-1]:
        blocks.append(swapped(local_kv, axis, bit))
    result = attend(query, blocks)
    return result.reshape(1, 1, tokens, queries.shape[3])


def solution(mesh):
    return jax.shard_map(
        per_device,
        mesh=mesh,
        in_specs=(P("ctxhi", "ctxlo", None, None), P("ctxhi", "ctxlo", None, None)),
        out_specs=P("ctxhi", "ctxlo", None, None),
        check_vma=False,
    )
```

```python
import math

import jax
import jax.numpy as jnp
from jax import lax
from jax.experimental import pallas as pl
from jax.sharding import PartitionSpec as P

HQ = 6
LAUNCH_ORDER = (
    ("ctxhi", 4), ("ctxlo", 3), ("ctxlo", 2), ("ctxhi", 3), ("ctxlo", 1),
    ("ctxhi", 2), ("ctxhi", 1), ("ctxlo", 0), ("ctxhi", 0),
)


def swapped(block, axis, stride):
    count = lax.axis_size(axis)
    route = []
    for low in range(count):
        high = low | 1 << stride
        if high != low and high < count:
            route += [(low, high), (high, low)]
    return lax.ppermute(block, axis, route)


def attend_kernel(*refs):
    q_ref = refs[0]
    kv_refs = refs[1:-1]
    o_ref = refs[-1]
    tokens = q_ref.shape[0]
    head_size = kv_refs[0].shape[1] // 2
    heads = q_ref.shape[1] // head_size
    scale = 1.0 / math.sqrt(head_size)
    query = jnp.concatenate(
        [q_ref[:, h * head_size:(h + 1) * head_size] for h in range(heads)], axis=0
    )
    scores = []
    top = None
    for kv_ref in kv_refs:
        block = lax.dot_general(
            kv_ref[:, :head_size], query, (((1,), (1,)), ((), ())),
            preferred_element_type=jnp.float32,
        )
        scores.append(block)
        block_top = jnp.max(block, axis=0, keepdims=True)
        top = block_top if top is None else jnp.maximum(top, block_top)
    summed = None
    total = None
    for kv_ref, block in zip(kv_refs, scores):
        expo = jnp.exp2((block - top) * (scale * math.log2(math.e)))
        block_total = jnp.sum(expo, axis=0, keepdims=True)
        total = block_total if total is None else total + block_total
        update = lax.dot_general(
            kv_ref[:, head_size:], expo.astype(jnp.bfloat16), (((0,), (0,)), ((), ())),
            preferred_element_type=jnp.float32,
        )
        summed = update if summed is None else summed + update
    result = (summed / total).T.astype(o_ref.dtype)
    for h in range(heads):
        o_ref[:, h * head_size:(h + 1) * head_size] = result[h * tokens:(h + 1) * tokens]


def attend(query, blocks):
    tokens, width = query.shape
    kv_spec = pl.BlockSpec(blocks[0].shape, lambda i: (0, 0))
    return pl.pallas_call(
        attend_kernel,
        out_shape=jax.ShapeDtypeStruct((tokens, width), jnp.bfloat16),
        grid=(1,),
        in_specs=[pl.BlockSpec((tokens, width), lambda i: (0, 0))] + [kv_spec] * len(blocks),
        out_specs=pl.BlockSpec((tokens, width), lambda i: (0, 0)),
    )(query, *blocks)


def per_device(key_value, queries):
    tokens = key_value.shape[2]
    pair = key_value.shape[3]
    local_kv = key_value.reshape(tokens, pair)
    query = queries.reshape(tokens, queries.shape[3])
    blocks = [local_kv]
    for axis, bit in LAUNCH_ORDER[::-1]:
        blocks.append(swapped(local_kv, axis, bit))
    result = attend(query, blocks)
    return result.reshape(1, 1, tokens, queries.shape[3])


def solution(mesh):
    return jax.shard_map(
        per_device,
        mesh=mesh,
        in_specs=(P("ctxhi", "ctxlo", None, None), P("ctxhi", "ctxlo", None, None)),
        out_specs=P("ctxhi", "ctxlo", None, None),
        check_vma=False,
    )
```
